256 devices in a mesh: pos: 64 (over x, y_hi, z), section: 4 (over y_lo, core).
Axes of the slice: x: 4, y: 4 (y_hi: 2, y_lo: 2; y = y_hi * 2 + y_lo), z: 8, core: 2. Of those that a mesh axis runs over, the one named last changes fastest.
Arguments:
- sequence_features: bfloat16 [262144, 128], P('pos'), may hold values from -6 to 6
- norm_gain: float32 [4, 2, 128], P('section'), may hold values from 0.5 to 2
- conv_weight: bfloat16 [4, 2, 3, 128, 128], P('section'), may hold values from -0.3125 to 0.3125
- conv_bias: float32 [4, 2, 128], P('section'), may hold values from -3 to 3
- mix_weight: bfloat16 [4, 2, 128, 128], P('section'), may hold values from -0.5 to 0.5
Outputs:
- section_outputs: bfloat16 [4, 262144, 128], P('section', 'pos')
The draws below stay inside these ranges and needn't reach their ends.
All inputs are finite; a program needn't handle non-finite values.
Results may differ from the reference program's by a relative error of at most 0.024.
Values may be sent and summed in bfloat16 or wider, within the bound.
No kernel may reach another device: no remote copies, remote signals or barrier semaphores. Data moves between devices by JAX's collectives and lax.ppermute only.
A program may use at most 64 MiB of HBM per device.

```python
import math
import jax
import jax.numpy as jnp
from jax import lax

C = 128
SECTION_LAYERS = 2
POSITIONS = 262144
BASE_DILATION = 32
N_SECTION = 4


def block_scale(stream_key, shape, shards, low, high):
    level = 1.0
    for position, blocks in shards:
        steps = jax.random.uniform(jax.random.fold_in(jax.random.fold_in(stream_key, 6), position), (blocks,), jnp.float32, low / len(shards), high / len(shards))
        level = level * jnp.repeat(jnp.exp(steps), shape[position] // blocks).reshape((-1,) + (1,) * (len(shape) - 1 - position))
    return level


def bell_draw(own_key, extent, deviation, most, split=(), kind=jnp.bfloat16):
    values = deviation * jax.random.normal(own_key, extent, jnp.float32)
    if split:
        values = values * block_scale(own_key, extent, split, -0.22, 0.18)
    return jnp.clip(values, -most, most).astype(kind)


def setup_inputs(seed: int = 0) -> dict:
    keys = jax.random.split(jax.random.key(seed), 6)
    return {
        "sequence_features": bell_draw(keys[0], (POSITIONS, C), 1.0, 6.0, ((0, 64),)),
        "norm_gain": jnp.clip(jnp.exp(math.log(2.0) - 1.3862944 * jax.random.uniform(keys[1], (N_SECTION, SECTION_LAYERS, C), jnp.float32) ** block_scale(keys[1], (N_SECTION, SECTION_LAYERS, C), ((0, 4),), -0.2, 0.2)), 0.5, 2.0),
        "conv_weight": bell_draw(keys[2], (N_SECTION, SECTION_LAYERS, 3, C, C), (3 * C) ** -0.5, 0.3125, ((0, 4),)),
        "conv_bias": bell_draw(keys[3], (N_SECTION, SECTION_LAYERS, C), 0.5, 3.0, ((0, 4),), jnp.float32),
        "mix_weight": bell_draw(keys[4], (N_SECTION, SECTION_LAYERS, C, C), C ** -0.5, 0.5, ((0, 4),)),
    }


def prepare(x, gain):
    r = x.astype(jnp.float32)
    meansq = lax.optimization_barrier(jnp.mean(r * r, axis=-1, keepdims=True))
    return jax.nn.gelu(r * lax.rsqrt(meansq + 1e-06) * gain, approximate=False).astype(jnp.bfloat16)

def reference(sequence_features, norm_gain, conv_weight, conv_bias, mix_weight):
    x = sequence_features
    results = []
    for section_index in range(N_SECTION):
        for layer_index in range(SECTION_LAYERS):
            dilation_factor = BASE_DILATION * 2 ** (section_index * SECTION_LAYERS + layer_index)
            h = prepare(x, norm_gain[section_index, layer_index])
            prior_layers = jnp.roll(h, dilation_factor, axis=0)
            after = jnp.roll(h, -dilation_factor, axis=0)
            conv = jnp.dot(prior_layers, conv_weight[section_index, layer_index, 0], preferred_element_type=jnp.float32)
            conv = conv + jnp.dot(h, conv_weight[section_index, layer_index, 1], preferred_element_type=jnp.float32)
            conv = conv + jnp.dot(after, conv_weight[section_index, layer_index, 2], preferred_element_type=jnp.float32)
            g = jax.nn.gelu(conv + conv_bias[section_index, layer_index], approximate=False).astype(jnp.bfloat16)
            x = (x.astype(jnp.float32) + jnp.dot(g, mix_weight[section_index, layer_index], preferred_element_type=jnp.float32)).astype(jnp.bfloat16)
        results.append(x)
    return jnp.stack(results)
```

```python
import jax
import jax.numpy as jnp
from jax import lax
from jax.sharding import PartitionSpec as P

RING = ("pos", "section")


def shifted(block, shift):
    count = lax.axis_size(RING)
    return lax.ppermute(block, RING, [(i, (i + shift) % count) for i in range(count)])


def prepare(x, gain):
    r = x.astype(jnp.float32)
    meansq = jnp.mean(r * r, axis=-1, keepdims=True)
    return jax.nn.gelu(r * lax.rsqrt(meansq + 1e-06) * gain, approximate=False).astype(jnp.bfloat16)


def layer(x, gain, taps, bias, mixing, dilation, chunk):
    h = prepare(x, gain)
    if dilation < chunk:
        before = jnp.concatenate([shifted(h[chunk - dilation :], 1), h[: chunk - dilation]], axis=0)
        after = jnp.concatenate([h[dilation:], shifted(h[:dilation], -1)], axis=0)
    else:
        hops = dilation // chunk
        before = shifted(h, hops)
        after = shifted(h, -hops)
    conv = jnp.dot(h, taps[1], preferred_element_type=jnp.float32)
    conv = conv + jnp.dot(before, taps[0], preferred_element_type=jnp.float32)
    conv = conv + jnp.dot(after, taps[2], preferred_element_type=jnp.float32)
    g = jax.nn.gelu(conv + bias, approximate=False).astype(jnp.bfloat16)
    return (x.astype(jnp.float32) + jnp.dot(g, mixing, preferred_element_type=jnp.float32)).astype(jnp.bfloat16)


def body(sequence_features, norm_gain, conv_weight, conv_bias, mix_weight):
    n_section = lax.axis_size("section")
    my_section = lax.axis_index("section")
    per_section = conv_weight.shape[1]
    block = sequence_features.shape[0]
    chunk = block // n_section
    first_dilation = block // 2 ** (per_section * n_section - 1)
    gains = lax.all_gather(norm_gain, "section", tiled=True)
    taps = lax.all_gather(conv_weight, "section", tiled=True)
    biases = lax.all_gather(conv_bias, "section", tiled=True)
    mixes = lax.all_gather(mix_weight, "section", tiled=True)
    x = lax.dynamic_slice_in_dim(sequence_features, my_section * chunk, chunk, axis=0)
    outs = []
    for step in range(n_section):
        for layer_index in range(per_section):
            dilation = first_dilation * 2 ** (step * per_section + layer_index)
            x = layer(
                x,
                gains[step, layer_index],
                taps[step, layer_index],
                biases[step, layer_index],
                mixes[step, layer_index],
                dilation,
                chunk,
            )
        outs.append(x)
    mine = lax.all_to_all(jnp.stack(outs), "section", 0, 0)
    return mine.reshape(1, block, mine.shape[-1])


def solution(mesh):
    in_specs = (
        P("pos", None),
        P("section", None, None),
        P("section", None, None, None, None),
        P("section", None, None),
        P("section", None, None, None),
    )
    out_specs = P("section", "pos", None)
    return jax.shard_map(body, mesh=mesh, in_specs=in_specs, out_specs=out_specs, check_vma=False)
```

```python
import jax
import jax.numpy as jnp
from jax import lax
from jax.sharding import PartitionSpec as P

REDUNDANT = 5


def shifted(block, shift):
    count = lax.axis_size("pos")
    return lax.ppermute(block, "pos", [(i, (i + shift) % count) for i in range(count)])


def prepare(x, gain):
    r = x.astype(jnp.float32)
    meansq = jnp.mean(r * r, axis=-1, keepdims=True)
    return jax.nn.gelu(r * lax.rsqrt(meansq + 1e-06) * gain, approximate=False).astype(jnp.bfloat16)


def mix(x, before, h, after, taps, bias, mixing):
    conv = jnp.dot(h, taps[1], preferred_element_type=jnp.float32)
    conv = conv + jnp.dot(before, taps[0], preferred_element_type=jnp.float32)
    conv = conv + jnp.dot(after, taps[2], preferred_element_type=jnp.float32)
    g = jax.nn.gelu(conv + bias, approximate=False).astype(jnp.bfloat16)
    return (x.astype(jnp.float32) + jnp.dot(g, mixing, preferred_element_type=jnp.float32)).astype(jnp.bfloat16)


def widened_layer(x, gain, taps, bias, mixing, shift):
    count = x.shape[0]
    h = prepare(x, gain)
    return mix(
        x[shift : count - shift], h[: count - 2 * shift], h[shift : count - shift], h[2 * shift :], taps, bias, mixing
    )


def exchanged_layer(x, gain, taps, bias, mixing, shift):
    chunk = x.shape[0]
    h = prepare(x, gain)
    if shift % chunk == 0:
        before = shifted(h, shift // chunk)
        after = shifted(h, -(shift // chunk))
    else:
        before = jnp.concatenate([shifted(h[chunk - shift :], 1), h[: chunk - shift]], axis=0)
        after = jnp.concatenate([h[shift:], shifted(h[:shift], -1)], axis=0)
    return mix(x, before, h, after, taps, bias, mixing)


def body(sequence_features, norm_gain, conv_weight, conv_bias, mix_weight):
    n_section = lax.axis_size("section")
    my_section = lax.axis_index("section")
    per_section = conv_weight.shape[1]
    block, channels = sequence_features.shape
    first_dilation = block // 2 ** (per_section * n_section - 1)
    group = first_dilation // n_section
    runs = block // first_dilation

    matrices = jnp.concatenate(
        [
            conv_weight.reshape(1, per_section * 3, channels, channels),
            mix_weight.reshape(1, per_section, channels, channels),
        ],
        axis=1,
    )
    vectors = jnp.concatenate([norm_gain, conv_bias], axis=1)
    matrices = lax.all_gather(matrices, "section", tiled=True)
    vectors = lax.all_gather(vectors, "section", tiled=True)

    runs_of = sequence_features.reshape(runs, n_section, group, channels)
    x = lax.dynamic_index_in_dim(runs_of, my_section, axis=1, keepdims=False).reshape(runs * group, channels)
    chunk = x.shape[0]

    shifts = [first_dilation * 2**index // n_section for index in range(per_section * n_section)]
    widen = sum(shifts[:REDUNDANT])
    assert widen <= chunk
    x = jnp.concatenate([shifted(x[chunk - widen :], 1), x, shifted(x[:widen], -1)], axis=0)

    result = None
    for index, shift in enumerate(shifts):
        step, layer_index = divmod(index, per_section)
        params = (
            vectors[step, layer_index],
            matrices[step, 3 * layer_index : 3 * layer_index + 3],
            vectors[step, per_section + layer_index],
            matrices[step, 3 * per_section + layer_index],
            shift,
        )
        if index < REDUNDANT:
            x = widened_layer(x, *params)
        else:
            x = exchanged_layer(x, *params)
        if layer_index == per_section - 1:
            edge = (x.shape[0] - chunk) // 2
            gathered = lax.all_gather(x[edge : edge + chunk], "section")
            result = gathered if result is None else jnp.where(my_section == step, gathered, result)
    result = result.reshape(n_section, runs, group, channels).transpose(1, 0, 2, 3)
    return result.reshape(1, block, channels)


def solution(mesh):
    in_specs = (
        P("pos", None),
        P("section", None, None),
        P("section", None, None, None, None),
        P("section", None, None),
        P("section", None, None, None),
    )
    out_specs = P("section", "pos", None)
    return jax.shard_map(body, mesh=mesh, in_specs=in_specs, out_specs=out_specs, check_vma=False)
```

```python
import jax
import jax.numpy as jnp
from jax import lax
from jax.sharding import PartitionSpec as P

REDUNDANT = 5


def shifted(block, shift):
    count = lax.axis_size("pos")
    return lax.ppermute(block, "pos", [(i, (i + shift) % count) for i in range(count)])


def from_every_section(piece, my_section):
    count = lax.axis_size("section")
    received = [piece] + [
        lax.ppermute(piece, "section", [(i, (i + hops) % count) for i in range(count)]) for hops in range(1, count)
    ]
    received = jnp.stack(received)
    return jnp.stack(
        [lax.dynamic_index_in_dim(received, (my_section - owner) % count, keepdims=False) for owner in range(count)]
    )


def to_one_section(piece, target):
    count = lax.axis_size("section")
    return jnp.stack(
        [
            piece if source == target else lax.ppermute(piece, "section", [(source, target)])
            for source in range(count)
        ]
    )


def prepare(x, gain):
    r = x.astype(jnp.float32)
    meansq = jnp.mean(r * r, axis=-1, keepdims=True)
    return jax.nn.gelu(r * lax.rsqrt(meansq + 1e-06) * gain, approximate=False).astype(jnp.bfloat16)


def mix(x, before, h, after, taps, bias, mixing):
    conv = jnp.dot(h, taps[1], preferred_element_type=jnp.float32)
    conv = conv + jnp.dot(before, taps[0], preferred_element_type=jnp.float32)
    conv = conv + jnp.dot(after, taps[2], preferred_element_type=jnp.float32)
    g = jax.nn.gelu(conv + bias, approximate=False).astype(jnp.bfloat16)
    return (x.astype(jnp.float32) + jnp.dot(g, mixing, preferred_element_type=jnp.float32)).astype(jnp.bfloat16)


def widened_layer(x, gain, taps, bias, mixing, shift):
    count = x.shape[0]
    h = prepare(x, gain)
    return mix(
        x[shift : count - shift], h[: count - 2 * shift], h[shift : count - shift], h[2 * shift :], taps, bias, mixing
    )


def exchanged_layer(x, gain, taps, bias, mixing, shift):
    chunk = x.shape[0]
    h = prepare(x, gain)
    if shift % chunk == 0:
        before = shifted(h, shift // chunk)
        after = shifted(h, -(shift // chunk))
    else:
        before = jnp.concatenate([shifted(h[chunk - shift :], 1), h[: chunk - shift]], axis=0)
        after = jnp.concatenate([h[shift:], shifted(h[:shift], -1)], axis=0)
    return mix(x, before, h, after, taps, bias, mixing)


def body(sequence_features, norm_gain, conv_weight, conv_bias, mix_weight):
    n_section = lax.axis_size("section")
    my_section = lax.axis_index("section")
    per_section = conv_weight.shape[1]
    block, channels = sequence_features.shape
    first_dilation = block // 2 ** (per_section * n_section - 1)
    group = first_dilation // n_section
    runs = block // first_dilation

    matrices = jnp.concatenate(
        [
            conv_weight.reshape(1, per_section * 3, channels, channels),
            mix_weight.reshape(1, per_section, channels, channels),
        ],
        axis=1,
    )
    vectors = jnp.concatenate([norm_gain, conv_bias], axis=1)
    matrices = from_every_section(matrices[0], my_section)
    vectors = from_every_section(vectors[0], my_section)

    runs_of = sequence_features.reshape(runs, n_section, group, channels)
    x = lax.dynamic_index_in_dim(runs_of, my_section, axis=1, keepdims=False).reshape(runs * group, channels)
    chunk = x.shape[0]

    shifts = [first_dilation * 2**index // n_section for index in range(per_section * n_section)]
    widen = sum(shifts[:REDUNDANT])
    assert widen <= chunk
    x = jnp.concatenate([shifted(x[chunk - widen :], 1), x, shifted(x[:widen], -1)], axis=0)

    result = None
    for index, shift in enumerate(shifts):
        step, layer_index = divmod(index, per_section)
        params = (
            vectors[step, layer_index],
            matrices[step, 3 * layer_index : 3 * layer_index + 3],
            vectors[step, per_section + layer_index],
            matrices[step, 3 * per_section + layer_index],
            shift,
        )
        if index < REDUNDANT:
            x = widened_layer(x, *params)
        else:
            x = exchanged_layer(x, *params)
        if layer_index == per_section - 1:
            edge = (x.shape[0] - chunk) // 2
            gathered = to_one_section(x[edge : edge + chunk], step)
            result = gathered if result is None else jnp.where(my_section == step, gathered, result)
    result = result.reshape(n_section, runs, group, channels).transpose(1, 0, 2, 3)
    return result.reshape(1, block, channels)


def solution(mesh):
    in_specs = (
        P("pos", None),
        P("section", None, None),
        P("section", None, None, None, None),
        P("section", None, None),
        P("section", None, None, None),
    )
    out_specs = P("section", "pos", None)
    return jax.shard_map(body, mesh=mesh, in_specs=in_specs, out_specs=out_specs, check_vma=False)
```

```python
import jax
import jax.numpy as jnp
from jax import lax
from jax.sharding import PartitionSpec as P

REDUNDANT = 5


def shifted(block, shift):
    count = lax.axis_size("pos")
    return lax.ppermute(block, "pos", [(i, (i + shift) % count) for i in range(count)])


def exact_bf16_parts(v):
    hi = v.astype(jnp.bfloat16)
    rest = v - hi.astype(jnp.float32)
    mid = rest.astype(jnp.bfloat16)
    lo = (rest - mid.astype(jnp.float32)).astype(jnp.bfloat16)
    return jnp.concatenate([hi, mid, lo], axis=0)


def from_shifts(piece, my_section):
    count = lax.axis_size("section")
    received = [piece] + [
        lax.ppermute(piece, "section", [(i, (i + hops) % count) for i in range(count)]) for hops in range(1, count)
    ]
    return jnp.stack(received)


def by_owner(received, my_section):
    count = received.shape[0]
    return jnp.stack(
        [lax.dynamic_index_in_dim(received, (my_section - owner) % count, keepdims=False) for owner in range(count)]
    )


def to_one_section(piece, target):
    count = lax.axis_size("section")
    return jnp.stack(
        [
            piece if source == target else lax.ppermute(piece, "section", [(source, target)])
            for source in range(count)
        ]
    )


def prepare(x, gain):
    r = x.astype(jnp.float32)
    meansq = jnp.mean(r * r, axis=-1, keepdims=True)
    return jax.nn.gelu(r * lax.rsqrt(meansq + 1e-06) * gain, approximate=False).astype(jnp.bfloat16)


def mix(x, before, h, after, taps, bias, mixing):
    conv = jnp.dot(h, taps[1], preferred_element_type=jnp.float32)
    conv = conv + jnp.dot(before, taps[0], preferred_element_type=jnp.float32)
    conv = conv + jnp.dot(after, taps[2], preferred_element_type=jnp.float32)
    g = jax.nn.gelu(conv + bias, approximate=False).astype(jnp.bfloat16)
    return (x.astype(jnp.float32) + jnp.dot(g, mixing, preferred_element_type=jnp.float32)).astype(jnp.bfloat16)


def widened_layer(x, gain, taps, bias, mixing, shift):
    count = x.shape[0]
    h = prepare(x, gain)
    return mix(
        x[shift : count - shift], h[: count - 2 * shift], h[shift : count - shift], h[2 * shift :], taps, bias, mixing
    )


def exchanged_layer(x, gain, taps, bias, mixing, shift):
    chunk = x.shape[0]
    h = prepare(x, gain)
    if shift % chunk == 0:
        before = shifted(h, shift // chunk)
        after = shifted(h, -(shift // chunk))
    else:
        before = jnp.concatenate([shifted(h[chunk - shift :], 1), h[: chunk - shift]], axis=0)
        after = jnp.concatenate([h[shift:], shifted(h[:shift], -1)], axis=0)
    return mix(x, before, h, after, taps, bias, mixing)


def body(sequence_features, norm_gain, conv_weight, conv_bias, mix_weight):
    n_section = lax.axis_size("section")
    my_section = lax.axis_index("section")
    per_section = conv_weight.shape[1]
    block, channels = sequence_features.shape
    first_dilation = block // 2 ** (per_section * n_section - 1)
    group = first_dilation // n_section
    runs = block // first_dilation

    matrices = jnp.concatenate(
        [
            conv_weight.reshape(1, per_section * 3, channels, channels),
            mix_weight.reshape(1, per_section, channels, channels),
        ],
        axis=1,
    )
    vectors = jnp.concatenate([norm_gain, conv_bias], axis=1)[0]

    runs_of = sequence_features.reshape(runs, n_section, group, channels)
    x = lax.dynamic_index_in_dim(runs_of, my_section, axis=1, keepdims=False).reshape(runs * group, channels)
    chunk = x.shape[0]

    shifts = [first_dilation * 2**index // n_section for index in range(per_section * n_section)]
    widen = sum(shifts[:REDUNDANT])
    assert widen <= chunk
    x = jnp.concatenate([shifted(x[chunk - widen :], 1), x, shifted(x[:widen], -1)], axis=0)

    n_matrix_rows = matrices.shape[1] * channels
    packed = jnp.concatenate([matrices[0].reshape(n_matrix_rows, channels), exact_bf16_parts(vectors)], axis=0)
    packed = by_owner(from_shifts(packed, my_section), my_section)
    matrices = packed[:, :n_matrix_rows].reshape(n_section, -1, channels, channels)
    parts = packed[:, n_matrix_rows:].astype(jnp.float32).reshape(n_section, 3, -1, channels)
    vectors = parts[:, 0] + parts[:, 1] + parts[:, 2]

    outs = []
    early = None
    for index, shift in enumerate(shifts):
        step, layer_index = divmod(index, per_section)
        params = (
            vectors[step, layer_index],
            matrices[step, 3 * layer_index : 3 * layer_index + 3],
            vectors[step, per_section + layer_index],
            matrices[step, 3 * per_section + layer_index],
            shift,
        )
        if index < REDUNDANT:
            x = widened_layer(x, *params)
        else:
            x = exchanged_layer(x, *params)
        if layer_index == per_section - 1:
            edge = (x.shape[0] - chunk) // 2
            outs.append(x[edge : edge + chunk])
        if len(outs) == n_section - 1 and early is None:
            outs_here = jnp.stack(outs + [outs[-1]])
            early = [
                lax.dynamic_index_in_dim(outs_here, (my_section + hops) % n_section, keepdims=False)
                for hops in range(n_section)
            ]
            early = [early[0]] + [
                lax.ppermute(early[hops], "section", [(i, (i + hops) % n_section) for i in range(n_section)])
                for hops in range(1, n_section)
            ]
            early = by_owner(jnp.stack(early), my_section)
    result = jnp.where(my_section == n_section - 1, to_one_section(outs[-1], n_section - 1), early)
    result = result.reshape(n_section, runs, group, channels).transpose(1, 0, 2, 3)
    return result.reshape(1, block, channels)


def solution(mesh):
    in_specs = (
        P("pos", None),
        P("section", None, None),
        P("section", None, None, None, None),
        P("section", None, None),
        P("section", None, None, None),
    )
    out_specs = P("section", "pos", None)
    return jax.shard_map(body, mesh=mesh, in_specs=in_specs, out_specs=out_specs, check_vma=False)
```

```python
import functools

import jax
import jax.numpy as jnp
from jax import lax
from jax.sharding import PartitionSpec as P

REDUNDANT = 5


def shifted(block, shift):
    count = lax.axis_size("pos")
    return lax.ppermute(block, "pos", [(i, (i + shift) % count) for i in range(count)])


def exact_bf16_parts(v):
    rest = v - lax.reduce_precision(v, exponent_bits=8, mantissa_bits=7)
    low = rest - lax.reduce_precision(rest, exponent_bits=8, mantissa_bits=7)
    return jnp.concatenate([part.astype(jnp.bfloat16) for part in (v, rest, low)], axis=0)


def weight_routes(mesh):
    devices = list(mesh.devices.reshape(-1))
    n_section = mesh.shape["section"]
    where = {(*d.coords, d.core_on_chip): i for i, d in enumerate(devices)}
    size_y = 1 + max(d.coords[1] for d in devices)
    first, second = [], []
    for i, d in enumerate(devices):
        x, y, z = d.coords
        core = d.core_on_chip
        step = 1 if (y % 2 == 0) == (core == 0) else -1
        first.append((where[(x, (y - step) % size_y, z, core)], i))
        second.append((where[(x, y, z, 1 - core)], i))
    source1 = {t: f for f, t in first}
    source2 = {t: f for f, t in second}
    table = []
    for i in range(len(devices)):
        order = [i, source1[i], source2[i], source1[source2[i]]]
        table.append([k % n_section for k in order])
    if any(row != [row[0] ^ code for code in (0, 2, 1, 3)] for row in table):
        return None
    return first, second


def routed_weights(piece, routes, my_section):
    first, second = routes
    ring = ("pos", "section")
    held = jnp.stack([piece, lax.ppermute(piece, ring, first)])
    held = jnp.concatenate([held, lax.ppermute(held, ring, second)], axis=0)
    picked = []
    for owner in range(held.shape[0]):
        code = my_section ^ owner
        picked.append(lax.dynamic_index_in_dim(held, (code & 1) * 2 + (code >> 1), keepdims=False))
    return jnp.stack(picked)


def from_shifts(piece, my_section):
    count = lax.axis_size("section")
    received = [piece] + [
        lax.ppermute(piece, "section", [(i, (i + hops) % count) for i in range(count)]) for hops in range(1, count)
    ]
    return jnp.stack(received)


def by_owner(received, my_section):
    count = received.shape[0]
    return jnp.stack(
        [lax.dynamic_index_in_dim(received, (my_section - owner) % count, keepdims=False) for owner in range(count)]
    )


def to_one_section(piece, target):
    count = lax.axis_size("section")
    return jnp.stack(
        [
            piece if source == target else lax.ppermute(piece, "section", [(source, target)])
            for source in range(count)
        ]
    )


def prepare(x, gain):
    r = x.astype(jnp.float32)
    meansq = jnp.mean(r * r, axis=-1, keepdims=True)
    return jax.nn.gelu(r * lax.rsqrt(meansq + 1e-06) * gain, approximate=False).astype(jnp.bfloat16)


def mix(x, before, h, after, taps, bias, mixing):
    conv = jnp.dot(h, taps[1], preferred_element_type=jnp.float32)
    conv = conv + jnp.dot(before, taps[0], preferred_element_type=jnp.float32)
    conv = conv + jnp.dot(after, taps[2], preferred_element_type=jnp.float32)
    g = jax.nn.gelu(conv + bias, approximate=False).astype(jnp.bfloat16)
    return (x.astype(jnp.float32) + jnp.dot(g, mixing, preferred_element_type=jnp.float32)).astype(jnp.bfloat16)


def widened_layer(x, gain, taps, bias, mixing, shift):
    count = x.shape[0]
    h = prepare(x, gain)
    return mix(
        x[shift : count - shift], h[: count - 2 * shift], h[shift : count - shift], h[2 * shift :], taps, bias, mixing
    )


def exchanged_layer(x, gain, taps, bias, mixing, shift):
    chunk = x.shape[0]
    h = prepare(x, gain)
    if shift % chunk == 0:
        before = shifted(h, shift // chunk)
        after = shifted(h, -(shift // chunk))
    else:
        before = jnp.concatenate([shifted(h[chunk - shift :], 1), h[: chunk - shift]], axis=0)
        after = jnp.concatenate([h[shift:], shifted(h[:shift], -1)], axis=0)
    return mix(x, before, h, after, taps, bias, mixing)


def body(routes, sequence_features, norm_gain, conv_weight, conv_bias, mix_weight):
    n_section = lax.axis_size("section")
    my_section = lax.axis_index("section")
    per_section = conv_weight.shape[1]
    block, channels = sequence_features.shape
    first_dilation = block // 2 ** (per_section * n_section - 1)
    group = first_dilation // n_section
    runs = block // first_dilation

    matrices = jnp.concatenate(
        [
            conv_weight.reshape(1, per_section * 3, channels, channels),
            mix_weight.reshape(1, per_section, channels, channels),
        ],
        axis=1,
    )
    vectors = jnp.concatenate([norm_gain, conv_bias], axis=1)[0]

    runs_of = sequence_features.reshape(runs, n_section, group, channels)
    x = lax.dynamic_index_in_dim(runs_of, my_section, axis=1, keepdims=False).reshape(runs * group, channels)
    chunk = x.shape[0]

    shifts = [first_dilation * 2**index // n_section for index in range(per_section * n_section)]
    widen = sum(shifts[:REDUNDANT])
    assert widen <= chunk
    x = jnp.concatenate([shifted(x[chunk - widen :], 1), x, shifted(x[:widen], -1)], axis=0)

    n_matrix_rows = matrices.shape[1] * channels
    packed = jnp.concatenate([matrices[0].reshape(n_matrix_rows, channels), exact_bf16_parts(vectors)], axis=0)
    if routes is None:
        packed = by_owner(from_shifts(packed, my_section), my_section)
    else:
        packed = routed_weights(packed, routes, my_section)
    matrices = packed[:, :n_matrix_rows].reshape(n_section, -1, channels, channels)
    parts = packed[:, n_matrix_rows:].astype(jnp.float32).reshape(n_section, 3, -1, channels)
    vectors = parts[:, 0] + parts[:, 1] + parts[:, 2]

    outs = []
    early = None
    for index, shift in enumerate(shifts):
        step, layer_index = divmod(index, per_section)
        params = (
            vectors[step, layer_index],
            matrices[step, 3 * layer_index : 3 * layer_index + 3],
            vectors[step, per_section + layer_index],
            matrices[step, 3 * per_section + layer_index],
            shift,
        )
        if index < REDUNDANT:
            x = widened_layer(x, *params)
        else:
            x = exchanged_layer(x, *params)
        if layer_index == per_section - 1:
            edge = (x.shape[0] - chunk) // 2
            outs.append(x[edge : edge + chunk])
        if len(outs) == n_section - 1 and early is None:
            outs_here = jnp.stack(outs + [outs[-1]])
            early = [
                lax.dynamic_index_in_dim(outs_here, (my_section + hops) % n_section, keepdims=False)
                for hops in range(n_section)
            ]
            early = [early[0]] + [
                lax.ppermute(early[hops], "section", [(i, (i + hops) % n_section) for i in range(n_section)])
                for hops in range(1, n_section)
            ]
            early = by_owner(jnp.stack(early), my_section)
    result = jnp.where(my_section == n_section - 1, to_one_section(outs[-1], n_section - 1), early)
    result = result.reshape(n_section, runs, group, channels).transpose(1, 0, 2, 3)
    return result.reshape(1, block, channels)


def solution(mesh):
    in_specs = (
        P("pos", None),
        P("section", None, None),
        P("section", None, None, None, None),
        P("section", None, None),
        P("section", None, None, None),
    )
    out_specs = P("section", "pos", None)
    routes = weight_routes(mesh) if mesh.shape["section"] == 4 else None
    return jax.shard_map(
        functools.partial(body, routes), mesh=mesh, in_specs=in_specs, out_specs=out_specs, check_vma=False
    )
```

```python
import functools

import jax
import jax.numpy as jnp
from jax import lax
from jax.sharding import PartitionSpec as P

REDUNDANT = 5


def shifted(block, shift):
    count = lax.axis_size("pos")
    return lax.ppermute(block, "pos", [(i, (i + shift) % count) for i in range(count)])


def exact_bf16_parts(v):
    rest = v - lax.reduce_precision(v, exponent_bits=8, mantissa_bits=7)
    low = rest - lax.reduce_precision(rest, exponent_bits=8, mantissa_bits=7)
    return jnp.concatenate([part.astype(jnp.bfloat16) for part in (v, rest, low)], axis=0)


def weight_routes(mesh):
    devices = list(mesh.devices.reshape(-1))
    n_section = mesh.shape["section"]
    where = {(*d.coords, d.core_on_chip): i for i, d in enumerate(devices)}
    size_y = 1 + max(d.coords[1] for d in devices)
    first, second = [], []
    for i, d in enumerate(devices):
        x, y, z = d.coords
        core = d.core_on_chip
        step = 1 if (y % 2 == 0) == (core == 0) else -1
        first.append((where[(x, (y - step) % size_y, z, core)], i))
        second.append((where[(x, y, z, 1 - core)], i))
    source1 = {t: f for f, t in first}
    source2 = {t: f for f, t in second}
    table = []
    for i in range(len(devices)):
        order = [i, source1[i], source2[i], source1[source2[i]]]
        table.append([k % n_section for k in order])
    if any(row != [row[0] ^ code for code in (0, 2, 1, 3)] for row in table):
        return None
    return first, second


def routed_weights(piece, routes, my_section):
    first, second = routes
    ring = ("pos", "section")
    across = lax.ppermute(piece, ring, first)
    held = [piece, across, lax.ppermute(piece, ring, second), lax.ppermute(across, ring, second)]
    picked = []
    for owner in range(len(held)):
        code = my_section ^ owner
        picked.append(lax.select_n((code & 1) * 2 + (code >> 1), *held))
    return jnp.stack(picked)


def from_shifts(piece, my_section):
    count = lax.axis_size("section")
    received = [piece] + [
        lax.ppermute(piece, "section", [(i, (i + hops) % count) for i in range(count)]) for hops in range(1, count)
    ]
    return jnp.stack(received)


def by_owner(received, my_section):
    count = received.shape[0]
    return jnp.stack(
        [lax.dynamic_index_in_dim(received, (my_section - owner) % count, keepdims=False) for owner in range(count)]
    )


def to_one_section(piece, target):
    count = lax.axis_size("section")
    return jnp.stack(
        [
            piece if source == target else lax.ppermute(piece, "section", [(source, target)])
            for source in range(count)
        ]
    )


def prepare(x, gain):
    r = x.astype(jnp.float32)
    meansq = jnp.mean(r * r, axis=-1, keepdims=True)
    return jax.nn.gelu(r * lax.rsqrt(meansq + 1e-06) * gain, approximate=False).astype(jnp.bfloat16)


def mix(x, before, h, after, taps, bias, mixing):
    conv = jnp.dot(h, taps[1], preferred_element_type=jnp.float32)
    conv = conv + jnp.dot(before, taps[0], preferred_element_type=jnp.float32)
    conv = conv + jnp.dot(after, taps[2], preferred_element_type=jnp.float32)
    g = jax.nn.gelu(conv + bias, approximate=False).astype(jnp.bfloat16)
    return (x.astype(jnp.float32) + jnp.dot(g, mixing, preferred_element_type=jnp.float32)).astype(jnp.bfloat16)


def widened_layer(x, gain, taps, bias, mixing, shift):
    count = x.shape[0]
    h = prepare(x, gain)
    return mix(
        x[shift : count - shift], h[: count - 2 * shift], h[shift : count - shift], h[2 * shift :], taps, bias, mixing
    )


def exchanged_layer(x, gain, taps, bias, mixing, shift):
    chunk = x.shape[0]
    h = prepare(x, gain)
    if shift % chunk == 0:
        before = shifted(h, shift // chunk)
        after = shifted(h, -(shift // chunk))
    else:
        before = jnp.concatenate([shifted(h[chunk - shift :], 1), h[: chunk - shift]], axis=0)
        after = jnp.concatenate([h[shift:], shifted(h[:shift], -1)], axis=0)
    return mix(x, before, h, after, taps, bias, mixing)


def body(routes, sequence_features, norm_gain, conv_weight, conv_bias, mix_weight):
    n_section = lax.axis_size("section")
    my_section = lax.axis_index("section")
    per_section = conv_weight.shape[1]
    block, channels = sequence_features.shape
    first_dilation = block // 2 ** (per_section * n_section - 1)
    group = first_dilation // n_section
    runs = block // first_dilation

    matrices = jnp.concatenate(
        [
            conv_weight.reshape(1, per_section * 3, channels, channels),
            mix_weight.reshape(1, per_section, channels, channels),
        ],
        axis=1,
    )
    vectors = jnp.concatenate([norm_gain, conv_bias], axis=1)[0]

    runs_of = sequence_features.reshape(runs, n_section, group, channels)
    x = lax.dynamic_index_in_dim(runs_of, my_section, axis=1, keepdims=False).reshape(runs * group, channels)
    chunk = x.shape[0]

    shifts = [first_dilation * 2**index // n_section for index in range(per_section * n_section)]
    widen = sum(shifts[:REDUNDANT])
    assert widen <= chunk
    x = jnp.concatenate([shifted(x[chunk - widen :], 1), x, shifted(x[:widen], -1)], axis=0)

    n_matrix_rows = matrices.shape[1] * channels
    parts = exact_bf16_parts(vectors)
    filler = jnp.zeros((-parts.shape[0] % 16, channels), jnp.bfloat16)
    packed = jnp.concatenate([matrices[0].reshape(n_matrix_rows, channels), parts, filler], axis=0)
    if routes is None:
        packed = by_owner(from_shifts(packed, my_section), my_section)
    else:
        packed = routed_weights(packed, routes, my_section)
    matrices = packed[:, :n_matrix_rows].reshape(n_section, -1, channels, channels)
    parts = packed[:, n_matrix_rows : n_matrix_rows + parts.shape[0]].astype(jnp.float32)
    parts = parts.reshape(n_section, 3, -1, channels)
    vectors = parts[:, 0] + parts[:, 1] + parts[:, 2]

    outs = []
    early = None
    for index, shift in enumerate(shifts):
        step, layer_index = divmod(index, per_section)
        params = (
            vectors[step, layer_index],
            matrices[step, 3 * layer_index : 3 * layer_index + 3],
            vectors[step, per_section + layer_index],
            matrices[step, 3 * per_section + layer_index],
            shift,
        )
        if index < REDUNDANT:
            x = widened_layer(x, *params)
        else:
            x = exchanged_layer(x, *params)
        if layer_index == per_section - 1:
            edge = (x.shape[0] - chunk) // 2
            outs.append(x[edge : edge + chunk])
        if len(outs) == n_section - 1 and early is None:
            outs_here = jnp.stack(outs + [outs[-1]])
            early = [
                lax.dynamic_index_in_dim(outs_here, (my_section + hops) % n_section, keepdims=False)
                for hops in range(n_section)
            ]
            early = [early[0]] + [
                lax.ppermute(early[hops], "section", [(i, (i + hops) % n_section) for i in range(n_section)])
                for hops in range(1, n_section)
            ]
            early = by_owner(jnp.stack(early), my_section)
    result = jnp.where(my_section == n_section - 1, to_one_section(outs[-1], n_section - 1), early)
    result = result.reshape(n_section, runs, group, channels).transpose(1, 0, 2, 3)
    return result.reshape(1, block, channels)


def solution(mesh):
    in_specs = (
        P("pos", None),
        P("section", None, None),
        P("section", None, None, None, None),
        P("section", None, None),
        P("section", None, None, None),
    )
    out_specs = P("section", "pos", None)
    routes = weight_routes(mesh) if mesh.shape["section"] == 4 else None
    return jax.shard_map(
        functools.partial(body, routes), mesh=mesh, in_specs=in_specs, out_specs=out_specs, check_vma=False
    )
```

```python
import jax
import jax.numpy as jnp
from jax import lax
from jax.sharding import PartitionSpec as P

REDUNDANT = 5


def shifted(block, shift):
    count = lax.axis_size("pos")
    return lax.ppermute(block, "pos", [(i, (i + shift) % count) for i in range(count)])


def exact_bf16_parts(v):
    rest = v - lax.reduce_precision(v, exponent_bits=8, mantissa_bits=7)
    low = rest - lax.reduce_precision(rest, exponent_bits=8, mantissa_bits=7)
    return jnp.concatenate([part.astype(jnp.bfloat16) for part in (v, rest, low)], axis=0)


def from_shifts(piece, my_section):
    count = lax.axis_size("section")
    received = [piece] + [
        lax.ppermute(piece, "section", [(i, (i + hops) % count) for i in range(count)]) for hops in range(1, count)
    ]
    return jnp.stack(received)


def by_owner(received, my_section):
    count = received.shape[0]
    return jnp.stack(
        [lax.dynamic_index_in_dim(received, (my_section - owner) % count, keepdims=False) for owner in range(count)]
    )


def to_one_section(piece, target):
    count = lax.axis_size("section")
    return jnp.stack(
        [
            piece if source == target else lax.ppermute(piece, "section", [(source, target)])
            for source in range(count)
        ]
    )


def prepare(x, gain):
    r = x.astype(jnp.float32)
    meansq = jnp.mean(r * r, axis=-1, keepdims=True)
    return jax.nn.gelu(r * lax.rsqrt(meansq + 1e-06) * gain, approximate=False).astype(jnp.bfloat16)


def mix(x, before, h, after, taps, bias, mixing):
    conv = jnp.dot(h, taps[1], preferred_element_type=jnp.float32)
    conv = conv + jnp.dot(before, taps[0], preferred_element_type=jnp.float32)
    conv = conv + jnp.dot(after, taps[2], preferred_element_type=jnp.float32)
    g = jax.nn.gelu(conv + bias, approximate=False).astype(jnp.bfloat16)
    return (x.astype(jnp.float32) + jnp.dot(g, mixing, preferred_element_type=jnp.float32)).astype(jnp.bfloat16)


def widened_layer(x, gain, taps, bias, mixing, shift):
    count = x.shape[0]
    h = prepare(x, gain)
    return mix(
        x[shift : count - shift], h[: count - 2 * shift], h[shift : count - shift], h[2 * shift :], taps, bias, mixing
    )


def exchanged_layer(x, gain, taps, bias, mixing, shift):
    chunk = x.shape[0]
    h = prepare(x, gain)
    if shift % chunk == 0:
        before = shifted(h, shift // chunk)
        after = shifted(h, -(shift // chunk))
    else:
        before = jnp.concatenate([shifted(h[chunk - shift :], 1), h[: chunk - shift]], axis=0)
        after = jnp.concatenate([h[shift:], shifted(h[:shift], -1)], axis=0)
    return mix(x, before, h, after, taps, bias, mixing)


def body(sequence_features, norm_gain, conv_weight, conv_bias, mix_weight):
    n_section = lax.axis_size("section")
    my_section = lax.axis_index("section")
    per_section = conv_weight.shape[1]
    block, channels = sequence_features.shape
    first_dilation = block // 2 ** (per_section * n_section - 1)
    group = first_dilation // n_section
    runs = block // first_dilation

    matrices = jnp.concatenate(
        [
            conv_weight.reshape(1, per_section * 3, channels, channels),
            mix_weight.reshape(1, per_section, channels, channels),
        ],
        axis=1,
    )
    vectors = jnp.concatenate([norm_gain, conv_bias], axis=1)[0]

    runs_of = sequence_features.reshape(runs, n_section, group, channels)
    x = lax.dynamic_index_in_dim(runs_of, my_section, axis=1, keepdims=False).reshape(runs * group, channels)
    chunk = x.shape[0]

    shifts = [first_dilation * 2**index // n_section for index in range(per_section * n_section)]
    widen = sum(shifts[:REDUNDANT])
    assert widen <= chunk
    x = jnp.concatenate([shifted(x[chunk - widen :], 1), x, shifted(x[:widen], -1)], axis=0)

    n_matrix_rows = matrices.shape[1] * channels
    packed = jnp.concatenate([matrices[0].reshape(n_matrix_rows, channels), exact_bf16_parts(vectors)], axis=0)
    packed = by_owner(from_shifts(packed, my_section), my_section)
    matrices = packed[:, :n_matrix_rows].reshape(n_section, -1, channels, channels)
    parts = packed[:, n_matrix_rows:].astype(jnp.float32).reshape(n_section, 3, -1, channels)
    vectors = parts[:, 0] + parts[:, 1] + parts[:, 2]

    outs = []
    early = None
    for index, shift in enumerate(shifts):
        step, layer_index = divmod(index, per_section)
        params = (
            vectors[step, layer_index],
            matrices[step, 3 * layer_index : 3 * layer_index + 3],
            vectors[step, per_section + layer_index],
            matrices[step, 3 * per_section + layer_index],
            shift,
        )
        if index < REDUNDANT:
            x = widened_layer(x, *params)
        else:
            x = exchanged_layer(x, *params)
        if layer_index == per_section - 1:
            edge = (x.shape[0] - chunk) // 2
            outs.append(x[edge : edge + chunk])
        if len(outs) == n_section - 1 and early is None:
            outs_here = jnp.stack(outs + [outs[-1]])
            early = [
                lax.dynamic_index_in_dim(outs_here, (my_section + hops) % n_section, keepdims=False)
                for hops in range(n_section)
            ]
            early = [early[0]] + [
                lax.ppermute(early[hops], "section", [(i, (i + hops) % n_section) for i in range(n_section)])
                for hops in range(1, n_section)
            ]
            early = by_owner(jnp.stack(early), my_section)
    result = jnp.where(my_section == n_section - 1, to_one_section(outs[-1], n_section - 1), early)
    result = result.reshape(n_section, runs, group, channels).transpose(1, 0, 2, 3)
    return result.reshape(1, block, channels)


def solution(mesh):
    in_specs = (
        P("pos", None),
        P("section", None, None),
        P("section", None, None, None, None),
        P("section", None, None),
        P("section", None, None, None),
    )
    out_specs = P("section", "pos", None)
    return jax.shard_map(body, mesh=mesh, in_specs=in_specs, out_specs=out_specs, check_vma=False)
```

```python
import jax
import jax.numpy as jnp
from jax import lax
from jax.sharding import PartitionSpec as P

REDUNDANT = 5


def shifted(block, shift):
    count = lax.axis_size("pos")
    return lax.ppermute(block, "pos", [(i, (i + shift) % count) for i in range(count)])


def exact_bf16_parts(v):
    rest = v - lax.reduce_precision(v, exponent_bits=8, mantissa_bits=7)
    low = rest - lax.reduce_precision(rest, exponent_bits=8, mantissa_bits=7)
    return jnp.concatenate([part.astype(jnp.bfloat16) for part in (v, rest, low)], axis=0)


def from_shifts(piece, my_section):
    count = lax.axis_size("section")
    received = [piece] + [
        lax.ppermute(piece, "section", [(i, (i + hops) % count) for i in range(count)]) for hops in range(1, count)
    ]
    return jnp.stack(received)


def by_owner(received, my_section):
    count = received.shape[0]
    return jnp.stack(
        [lax.dynamic_index_in_dim(received, (my_section - owner) % count, keepdims=False) for owner in range(count)]
    )


def to_one_section(piece, target):
    count = lax.axis_size("section")
    return jnp.stack(
        [
            piece if source == target else lax.ppermute(piece, "section", [(source, target)])
            for source in range(count)
        ]
    )


def prepare(x, gain):
    r = x.astype(jnp.float32)
    meansq = jnp.mean(r * r, axis=-1, keepdims=True)
    return jax.nn.gelu(r * lax.rsqrt(meansq + 1e-06) * gain, approximate=False).astype(jnp.bfloat16)


def mix(x, before, h, after, taps, bias, mixing):
    conv = jnp.dot(h, taps[1], preferred_element_type=jnp.float32)
    conv = conv + jnp.dot(before, taps[0], preferred_element_type=jnp.float32)
    conv = conv + jnp.dot(after, taps[2], preferred_element_type=jnp.float32)
    g = jax.nn.gelu(conv + bias, approximate=False).astype(jnp.bfloat16)
    return (x.astype(jnp.float32) + jnp.dot(g, mixing, preferred_element_type=jnp.float32)).astype(jnp.bfloat16)


def widened_layer(x, gain, taps, bias, mixing, shift):
    count = x.shape[0]
    h = prepare(x, gain)
    return mix(
        x[shift : count - shift], h[: count - 2 * shift], h[shift : count - shift], h[2 * shift :], taps, bias, mixing
    )


def exchanged_layer(x, gain, taps, bias, mixing, shift):
    chunk = x.shape[0]
    h = prepare(x, gain)
    if shift % chunk == 0:
        before = shifted(h, shift // chunk)
        after = shifted(h, -(shift // chunk))
    else:
        before = jnp.concatenate([shifted(h[chunk - shift :], 1), h[: chunk - shift]], axis=0)
        after = jnp.concatenate([h[shift:], shifted(h[:shift], -1)], axis=0)
    return mix(x, before, h, after, taps, bias, mixing)


def body(sequence_features, norm_gain, conv_weight, conv_bias, mix_weight):
    n_section = lax.axis_size("section")
    my_section = lax.axis_index("section")
    per_section = conv_weight.shape[1]
    block, channels = sequence_features.shape
    first_dilation = block // 2 ** (per_section * n_section - 1)
    group = first_dilation // n_section
    runs = block // first_dilation

    matrices = jnp.concatenate(
        [
            conv_weight.reshape(1, per_section * 3, channels, channels),
            mix_weight.reshape(1, per_section, channels, channels),
        ],
        axis=1,
    )
    vectors = jnp.concatenate([norm_gain, conv_bias], axis=1)[0]

    runs_of = sequence_features.reshape(runs, n_section, group, channels)
    x = lax.dynamic_index_in_dim(runs_of, my_section, axis=1, keepdims=False).reshape(runs * group, channels)
    chunk = x.shape[0]

    shifts = [first_dilation * 2**index // n_section for index in range(per_section * n_section)]
    widen = sum(shifts[:REDUNDANT])
    assert widen <= chunk
    x = jnp.concatenate([shifted(x[chunk - widen :], 1), x, shifted(x[:widen], -1)], axis=0)

    n_matrix_rows = matrices.shape[1] * channels
    packed = jnp.concatenate([matrices[0].reshape(n_matrix_rows, channels), exact_bf16_parts(vectors)], axis=0)
    packed = by_owner(from_shifts(packed, my_section), my_section)
    matrices = packed[:, :n_matrix_rows].reshape(n_section, -1, channels, channels)
    parts = packed[:, n_matrix_rows:].astype(jnp.float32).reshape(n_section, 3, -1, channels)
    vectors = parts[:, 0] + parts[:, 1] + parts[:, 2]

    outs = []
    for index, shift in enumerate(shifts):
        step, layer_index = divmod(index, per_section)
        params = (
            vectors[step, layer_index],
            matrices[step, 3 * layer_index : 3 * layer_index + 3],
            vectors[step, per_section + layer_index],
            matrices[step, 3 * per_section + layer_index],
            shift,
        )
        if index < REDUNDANT:
            x = widened_layer(x, *params)
        else:
            x = exchanged_layer(x, *params)
        if layer_index == per_section - 1:
            edge = (x.shape[0] - chunk) // 2
            outs.append(x[edge : edge + chunk])
    outs_here = jnp.stack(outs)
    sent = [
        lax.dynamic_index_in_dim(outs_here, (my_section + hops) % n_section, keepdims=False) for hops in range(n_section)
    ]
    sent = [sent[0]] + [
        lax.ppermute(sent[hops], "section", [(i, (i + hops) % n_section) for i in range(n_section)])
        for hops in range(1, n_section)
    ]
    result = by_owner(jnp.stack(sent), my_section)
    result = result.reshape(n_section, runs, group, channels).transpose(1, 0, 2, 3)
    return result.reshape(1, block, channels)


def solution(mesh):
    in_specs = (
        P("pos", None),
        P("section", None, None),
        P("section", None, None, None, None),
        P("section", None, None),
        P("section", None, None, None),
    )
    out_specs = P("section", "pos", None)
    return jax.shard_map(body, mesh=mesh, in_specs=in_specs, out_specs=out_specs, check_vma=False)
```

```python
import jax
import jax.numpy as jnp
from jax import lax
from jax.sharding import PartitionSpec as P

REDUNDANT = 5


def shifted(block, shift):
    count = lax.axis_size("pos")
    return lax.ppermute(block, "pos", [(i, (i + shift) % count) for i in range(count)])


def exact_bf16_parts(v):
    rest = v - lax.reduce_precision(v, exponent_bits=8, mantissa_bits=7)
    low = rest - lax.reduce_precision(rest, exponent_bits=8, mantissa_bits=7)
    return jnp.concatenate([part.astype(jnp.bfloat16) for part in (v, rest, low)], axis=0)


def from_shifts(piece, my_section):
    count = lax.axis_size("section")
    received = [piece] + [
        lax.ppermute(piece, "section", [(i, (i + hops) % count) for i in range(count)]) for hops in range(1, count)
    ]
    return jnp.stack(received)


def by_owner(received, my_section):
    count = received.shape[0]
    return jnp.stack(
        [lax.dynamic_index_in_dim(received, (my_section - owner) % count, keepdims=False) for owner in range(count)]
    )


def to_one_section(piece, target):
    count = lax.axis_size("section")
    return jnp.stack(
        [
            piece if source == target else lax.ppermute(piece, "section", [(source, target)])
            for source in range(count)
        ]
    )


def prepare(x, gain):
    r = x.astype(jnp.float32)
    meansq = jnp.mean(r * r, axis=-1, keepdims=True)
    return jax.nn.gelu(r * lax.rsqrt(meansq + 1e-06) * gain, approximate=False).astype(jnp.bfloat16)


def mix(x, before, h, after, taps, bias, mixing):
    conv = jnp.dot(h, taps[1], preferred_element_type=jnp.float32)
    conv = conv + jnp.dot(before, taps[0], preferred_element_type=jnp.float32)
    conv = conv + jnp.dot(after, taps[2], preferred_element_type=jnp.float32)
    g = jax.nn.gelu(conv + bias, approximate=False).astype(jnp.bfloat16)
    return (x.astype(jnp.float32) + jnp.dot(g, mixing, preferred_element_type=jnp.float32)).astype(jnp.bfloat16)


def widened_layer(x, gain, taps, bias, mixing, shift):
    count = x.shape[0]
    h = prepare(x, gain)
    return mix(
        x[shift : count - shift], h[: count - 2 * shift], h[shift : count - shift], h[2 * shift :], taps, bias, mixing
    )


def exchanged_layer(x, gain, taps, bias, mixing, shift):
    chunk = x.shape[0]
    h = prepare(x, gain)
    if shift % chunk == 0:
        before = shifted(h, shift // chunk)
        after = shifted(h, -(shift // chunk))
    else:
        before = jnp.concatenate([shifted(h[chunk - shift :], 1), h[: chunk - shift]], axis=0)
        after = jnp.concatenate([h[shift:], shifted(h[:shift], -1)], axis=0)
    return mix(x, before, h, after, taps, bias, mixing)


def body(sequence_features, norm_gain, conv_weight, conv_bias, mix_weight):
    n_section = lax.axis_size("section")
    my_section = lax.axis_index("section")
    per_section = conv_weight.shape[1]
    block, channels = sequence_features.shape
    first_dilation = block // 2 ** (per_section * n_section - 1)
    group = first_dilation // n_section
    runs = block // first_dilation

    matrices = jnp.concatenate(
        [
            conv_weight.reshape(1, per_section * 3, channels, channels),
            mix_weight.reshape(1, per_section, channels, channels),
        ],
        axis=1,
    )
    vectors = jnp.concatenate([norm_gain, conv_bias], axis=1)[0]

    runs_of = sequence_features.reshape(runs, n_section, group, channels)
    x = lax.dynamic_index_in_dim(runs_of, my_section, axis=1, keepdims=False).reshape(runs * group, channels)
    chunk = x.shape[0]

    shifts = [first_dilation * 2**index // n_section for index in range(per_section * n_section)]
    widen = sum(shifts[:REDUNDANT])
    assert widen <= chunk
    x = jnp.concatenate([shifted(x[chunk - widen :], 1), x, shifted(x[:widen], -1)], axis=0)

    n_matrix_rows = matrices.shape[1] * channels
    packed = jnp.concatenate([matrices[0].reshape(n_matrix_rows, channels), exact_bf16_parts(vectors)], axis=0)
    packed = by_owner(from_shifts(packed, my_section), my_section)
    matrices = packed[:, :n_matrix_rows].reshape(n_section, -1, channels, channels)
    parts = packed[:, n_matrix_rows:].astype(jnp.float32).reshape(n_section, 3, -1, channels)
    vectors = parts[:, 0] + parts[:, 1] + parts[:, 2]

    outs = []
    for index, shift in enumerate(shifts):
        step, layer_index = divmod(index, per_section)
        params = (
            vectors[step, layer_index],
            matrices[step, 3 * layer_index : 3 * layer_index + 3],
            vectors[step, per_section + layer_index],
            matrices[step, 3 * per_section + layer_index],
            shift,
        )
        if index < REDUNDANT:
            x = widened_layer(x, *params)
        else:
            x = exchanged_layer(x, *params)
        if layer_index == per_section - 1:
            edge = (x.shape[0] - chunk) // 2
            outs.append(x[edge : edge + chunk])
    sent = [lax.select_n((my_section + hops) % n_section, *outs) for hops in range(n_section)]
    sent = [sent[0]] + [
        lax.ppermute(sent[hops], "section", [(i, (i + hops) % n_section) for i in range(n_section)])
        for hops in range(1, n_section)
    ]
    sent = [piece.reshape(runs, group, channels) for piece in sent]
    result = jnp.stack(
        [lax.select_n((my_section - owner) % n_section, *sent) for owner in range(n_section)], axis=1
    )
    return result.reshape(1, block, channels)


def solution(mesh):
    in_specs = (
        P("pos", None),
        P("section", None, None),
        P("section", None, None, None, None),
        P("section", None, None),
        P("section", None, None, None),
    )
    out_specs = P("section", "pos", None)
    return jax.shard_map(body, mesh=mesh, in_specs=in_specs, out_specs=out_specs, check_vma=False)
```

```python
import jax
import jax.numpy as jnp
from jax import lax
from jax.sharding import PartitionSpec as P

REDUNDANT = 6


def shifted(block, shift):
    count = lax.axis_size("pos")
    return lax.ppermute(block, "pos", [(i, (i + shift) % count) for i in range(count)])


def exact_bf16_parts(v):
    rest = v - lax.reduce_precision(v, exponent_bits=8, mantissa_bits=7)
    low = rest - lax.reduce_precision(rest, exponent_bits=8, mantissa_bits=7)
    return jnp.concatenate([part.astype(jnp.bfloat16) for part in (v, rest, low)], axis=0)


def from_shifts(piece, my_section):
    count = lax.axis_size("section")
    received = [piece] + [
        lax.ppermute(piece, "section", [(i, (i + hops) % count) for i in range(count)]) for hops in range(1, count)
    ]
    return jnp.stack(received)


def by_owner(received, my_section):
    count = received.shape[0]
    return jnp.stack(
        [lax.dynamic_index_in_dim(received, (my_section - owner) % count, keepdims=False) for owner in range(count)]
    )


def to_one_section(piece, target):
    count = lax.axis_size("section")
    return jnp.stack(
        [
            piece if source == target else lax.ppermute(piece, "section", [(source, target)])
            for source in range(count)
        ]
    )


def prepare(x, gain):
    r = x.astype(jnp.float32)
    meansq = jnp.mean(r * r, axis=-1, keepdims=True)
    return jax.nn.gelu(r * lax.rsqrt(meansq + 1e-06) * gain, approximate=False).astype(jnp.bfloat16)


def mix(x, before, h, after, taps, bias, mixing):
    conv = jnp.dot(h, taps[1], preferred_element_type=jnp.float32)
    conv = conv + jnp.dot(before, taps[0], preferred_element_type=jnp.float32)
    conv = conv + jnp.dot(after, taps[2], preferred_element_type=jnp.float32)
    g = jax.nn.gelu(conv + bias, approximate=False).astype(jnp.bfloat16)
    return (x.astype(jnp.float32) + jnp.dot(g, mixing, preferred_element_type=jnp.float32)).astype(jnp.bfloat16)


def widened_layer(x, gain, taps, bias, mixing, shift):
    count = x.shape[0]
    h = prepare(x, gain)
    return mix(
        x[shift : count - shift], h[: count - 2 * shift], h[shift : count - shift], h[2 * shift :], taps, bias, mixing
    )


def exchanged_layer(x, gain, taps, bias, mixing, shift):
    chunk = x.shape[0]
    h = prepare(x, gain)
    if shift % chunk == 0:
        before = shifted(h, shift // chunk)
        after = shifted(h, -(shift // chunk))
    else:
        before = jnp.concatenate([shifted(h[chunk - shift :], 1), h[: chunk - shift]], axis=0)
        after = jnp.concatenate([h[shift:], shifted(h[:shift], -1)], axis=0)
    return mix(x, before, h, after, taps, bias, mixing)


def body(sequence_features, norm_gain, conv_weight, conv_bias, mix_weight):
    n_section = lax.axis_size("section")
    my_section = lax.axis_index("section")
    per_section = conv_weight.shape[1]
    block, channels = sequence_features.shape
    first_dilation = block // 2 ** (per_section * n_section - 1)
    group = first_dilation // n_section
    runs = block // first_dilation

    matrices = jnp.concatenate(
        [
            conv_weight.reshape(1, per_section * 3, channels, channels),
            mix_weight.reshape(1, per_section, channels, channels),
        ],
        axis=1,
    )
    vectors = jnp.concatenate([norm_gain, conv_bias], axis=1)[0]

    runs_of = sequence_features.reshape(runs, n_section, group, channels)
    x = lax.dynamic_index_in_dim(runs_of, my_section, axis=1, keepdims=False).reshape(runs * group, channels)
    chunk = x.shape[0]

    shifts = [first_dilation * 2**index // n_section for index in range(per_section * n_section)]
    widen = sum(shifts[:REDUNDANT])
    assert widen <= chunk
    x = jnp.concatenate([shifted(x[chunk - widen :], 1), x, shifted(x[:widen], -1)], axis=0)

    n_matrix_rows = matrices.shape[1] * channels
    packed = jnp.concatenate([matrices[0].reshape(n_matrix_rows, channels), exact_bf16_parts(vectors)], axis=0)
    packed = by_owner(from_shifts(packed, my_section), my_section)
    matrices = packed[:, :n_matrix_rows].reshape(n_section, -1, channels, channels)
    parts = packed[:, n_matrix_rows:].astype(jnp.float32).reshape(n_section, 3, -1, channels)
    vectors = parts[:, 0] + parts[:, 1] + parts[:, 2]

    outs = []
    for index, shift in enumerate(shifts):
        step, layer_index = divmod(index, per_section)
        params = (
            vectors[step, layer_index],
            matrices[step, 3 * layer_index : 3 * layer_index + 3],
            vectors[step, per_section + layer_index],
            matrices[step, 3 * per_section + layer_index],
            shift,
        )
        if index < REDUNDANT:
            x = widened_layer(x, *params)
        else:
            x = exchanged_layer(x, *params)
        if layer_index == per_section - 1:
            edge = (x.shape[0] - chunk) // 2
            outs.append(x[edge : edge + chunk])
    outs_here = jnp.stack(outs)
    sent = [
        lax.dynamic_index_in_dim(outs_here, (my_section + hops) % n_section, keepdims=False) for hops in range(n_section)
    ]
    sent = [sent[0]] + [
        lax.ppermute(sent[hops], "section", [(i, (i + hops) % n_section) for i in range(n_section)])
        for hops in range(1, n_section)
    ]
    result = by_owner(jnp.stack(sent), my_section)
    result = result.reshape(n_section, runs, group, channels).transpose(1, 0, 2, 3)
    return result.reshape(1, block, channels)


def solution(mesh):
    in_specs = (
        P("pos", None),
        P("section", None, None),
        P("section", None, None, None, None),
        P("section", None, None),
        P("section", None, None, None),
    )
    out_specs = P("section", "pos", None)
    return jax.shard_map(body, mesh=mesh, in_specs=in_specs, out_specs=out_specs, check_vma=False)
```

```python
import functools

import jax
import jax.numpy as jnp
from jax import lax
from jax.sharding import PartitionSpec as P

REDUNDANT = 5


def shifted(block, shift):
    count = lax.axis_size("pos")
    return lax.ppermute(block, "pos", [(i, (i + shift) % count) for i in range(count)])


def exact_bf16_parts(v):
    rest = v - lax.reduce_precision(v, exponent_bits=8, mantissa_bits=7)
    low = rest - lax.reduce_precision(rest, exponent_bits=8, mantissa_bits=7)
    return jnp.concatenate([part.astype(jnp.bfloat16) for part in (v, rest, low)], axis=0)


def weight_routes(mesh):
    devices = list(mesh.devices.reshape(-1))
    n_section = mesh.shape["section"]
    where = {(*d.coords, d.core_on_chip): i for i, d in enumerate(devices)}
    size_y = 1 + max(d.coords[1] for d in devices)
    first, second = [], []
    for i, d in enumerate(devices):
        x, y, z = d.coords
        core = d.core_on_chip
        step = 1 if (y % 2 == 0) == (core == 0) else -1
        first.append((where[(x, (y - step) % size_y, z, core)], i))
        second.append((where[(x, y, z, 1 - core)], i))
    source1 = {t: f for f, t in first}
    source2 = {t: f for f, t in second}
    table = []
    for i in range(len(devices)):
        order = [i, source1[i], source2[i], source1[source2[i]]]
        table.append([k % n_section for k in order])
    if any(row != [row[0] ^ code for code in (0, 2, 1, 3)] for row in table):
        return None
    return first, second


def routed_weights(piece, routes, my_section):
    first, second = routes
    ring = ("pos", "section")
    across = lax.ppermute(piece, ring, first)
    held = [piece, across, lax.ppermute(piece, ring, second), lax.ppermute(across, ring, second)]
    picked = []
    for owner in range(len(held)):
        code = my_section ^ owner
        picked.append(lax.select_n((code & 1) * 2 + (code >> 1), *held))
    return jnp.stack(picked)


def from_shifts(piece, my_section):
    count = lax.axis_size("section")
    received = [piece] + [
        lax.ppermute(piece, "section", [(i, (i + hops) % count) for i in range(count)]) for hops in range(1, count)
    ]
    return jnp.stack(received)


def by_owner(received, my_section):
    count = received.shape[0]
    return jnp.stack(
        [lax.dynamic_index_in_dim(received, (my_section - owner) % count, keepdims=False) for owner in range(count)]
    )


def to_one_section(piece, target):
    count = lax.axis_size("section")
    return jnp.stack(
        [
            piece if source == target else lax.ppermute(piece, "section", [(source, target)])
            for source in range(count)
        ]
    )


def prepare(x, gain):
    r = x.astype(jnp.float32)
    meansq = jnp.mean(r * r, axis=-1, keepdims=True)
    return jax.nn.gelu(r * lax.rsqrt(meansq + 1e-06) * gain, approximate=False).astype(jnp.bfloat16)


def mix(x, before, h, after, taps, bias, mixing):
    conv = jnp.dot(h, taps[1], preferred_element_type=jnp.float32)
    conv = conv + jnp.dot(before, taps[0], preferred_element_type=jnp.float32)
    conv = conv + jnp.dot(after, taps[2], preferred_element_type=jnp.float32)
    g = jax.nn.gelu(conv + bias, approximate=False).astype(jnp.bfloat16)
    return (x.astype(jnp.float32) + jnp.dot(g, mixing, preferred_element_type=jnp.float32)).astype(jnp.bfloat16)


def widened_layer(x, gain, taps, bias, mixing, shift):
    count = x.shape[0]
    h = prepare(x, gain)
    return mix(
        x[shift : count - shift], h[: count - 2 * shift], h[shift : count - shift], h[2 * shift :], taps, bias, mixing
    )


def exchanged_layer(x, gain, taps, bias, mixing, shift):
    chunk = x.shape[0]
    h = prepare(x, gain)
    if shift % chunk == 0:
        before = shifted(h, shift // chunk)
        after = shifted(h, -(shift // chunk))
    else:
        before = jnp.concatenate([shifted(h[chunk - shift :], 1), h[: chunk - shift]], axis=0)
        after = jnp.concatenate([h[shift:], shifted(h[:shift], -1)], axis=0)
    return mix(x, before, h, after, taps, bias, mixing)


def body(routes, sequence_features, norm_gain, conv_weight, conv_bias, mix_weight):
    n_section = lax.axis_size("section")
    my_section = lax.axis_index("section")
    per_section = conv_weight.shape[1]
    block, channels = sequence_features.shape
    first_dilation = block // 2 ** (per_section * n_section - 1)
    group = first_dilation // n_section
    runs = block // first_dilation

    matrices = jnp.concatenate(
        [
            conv_weight.reshape(1, per_section * 3, channels, channels),
            mix_weight.reshape(1, per_section, channels, channels),
        ],
        axis=1,
    )
    vectors = jnp.concatenate([norm_gain, conv_bias], axis=1)[0]

    runs_of = sequence_features.reshape(runs, n_section, group, channels)
    x = lax.dynamic_index_in_dim(runs_of, my_section, axis=1, keepdims=False).reshape(runs * group, channels)
    chunk = x.shape[0]

    shifts = [first_dilation * 2**index // n_section for index in range(per_section * n_section)]
    widen = sum(shifts[:REDUNDANT])
    assert widen <= chunk
    x = jnp.concatenate([shifted(x[chunk - widen :], 1), x, shifted(x[:widen], -1)], axis=0)

    n_matrix_rows = matrices.shape[1] * channels
    parts = exact_bf16_parts(vectors)
    filler = jnp.zeros((-parts.shape[0] % 16, channels), jnp.bfloat16)
    packed = jnp.concatenate([matrices[0].reshape(n_matrix_rows, channels), parts, filler], axis=0)
    if routes is None:
        packed = by_owner(from_shifts(packed, my_section), my_section)
    else:
        packed = routed_weights(packed, routes, my_section)
    matrices = packed[:, :n_matrix_rows].reshape(n_section, -1, channels, channels)
    parts = packed[:, n_matrix_rows : n_matrix_rows + parts.shape[0]].astype(jnp.float32)
    parts = parts.reshape(n_section, 3, -1, channels)
    vectors = parts[:, 0] + parts[:, 1] + parts[:, 2]

    outs = []
    for index, shift in enumerate(shifts):
        step, layer_index = divmod(index, per_section)
        params = (
            vectors[step, layer_index],
            matrices[step, 3 * layer_index : 3 * layer_index + 3],
            vectors[step, per_section + layer_index],
            matrices[step, 3 * per_section + layer_index],
            shift,
        )
        if index < REDUNDANT:
            x = widened_layer(x, *params)
        else:
            x = exchanged_layer(x, *params)
        if layer_index == per_section - 1:
            edge = (x.shape[0] - chunk) // 2
            outs.append(x[edge : edge + chunk])
    outs_here = jnp.stack(outs)
    sent = [
        lax.dynamic_index_in_dim(outs_here, (my_section + hops) % n_section, keepdims=False) for hops in range(n_section)
    ]
    sent = [sent[0]] + [
        lax.ppermute(sent[hops], "section", [(i, (i + hops) % n_section) for i in range(n_section)])
        for hops in range(1, n_section)
    ]
    result = by_owner(jnp.stack(sent), my_section)
    result = result.reshape(n_section, runs, group, channels).transpose(1, 0, 2, 3)
    return result.reshape(1, block, channels)


def solution(mesh):
    in_specs = (
        P("pos", None),
        P("section", None, None),
        P("section", None, None, None, None),
        P("section", None, None),
        P("section", None, None, None),
    )
    out_specs = P("section", "pos", None)
    routes = weight_routes(mesh) if mesh.shape["section"] == 4 else None
    return jax.shard_map(
        functools.partial(body, routes), mesh=mesh, in_specs=in_specs, out_specs=out_specs, check_vma=False
    )
```

```python
import functools

import jax
import jax.numpy as jnp
from jax import lax
from jax.sharding import PartitionSpec as P

REDUNDANT = 5


def shifted(block, shift):
    count = lax.axis_size("pos")
    return lax.ppermute(block, "pos", [(i, (i + shift) % count) for i in range(count)])


def exact_bf16_parts(v):
    rest = v - lax.reduce_precision(v, exponent_bits=8, mantissa_bits=7)
    low = rest - lax.reduce_precision(rest, exponent_bits=8, mantissa_bits=7)
    return jnp.concatenate([part.astype(jnp.bfloat16) for part in (v, rest, low)], axis=0)


def weight_routes(mesh):
    devices = list(mesh.devices.reshape(-1))
    n_section = mesh.shape["section"]
    where = {(*d.coords, d.core_on_chip): i for i, d in enumerate(devices)}
    size_y = 1 + max(d.coords[1] for d in devices)
    first, second = [], []
    for i, d in enumerate(devices):
        x, y, z = d.coords
        core = d.core_on_chip
        step = 1 if (y % 2 == 0) == (core == 0) else -1
        first.append((where[(x, (y - step) % size_y, z, core)], i))
        second.append((where[(x, y, z, 1 - core)], i))
    source1 = {t: f for f, t in first}
    source2 = {t: f for f, t in second}
    table = []
    for i in range(len(devices)):
        order = [i, source1[i], source2[i], source1[source2[i]]]
        table.append([k % n_section for k in order])
    if any(row != [row[0] ^ code for code in (0, 2, 1, 3)] for row in table):
        return None
    return first, second


def halo_routes(mesh):
    devices = list(mesh.devices.reshape(-1))
    n_pos, n_section = mesh.shape["pos"], mesh.shape["section"]
    where = {(*d.coords, d.core_on_chip): i for i, d in enumerate(devices)}
    core_of = [devices[s].core_on_chip for s in range(n_section)]
    partner_of = [where[(*devices[s].coords, 1 - core_of[s])] % n_section for s in range(n_section)]
    along, across = [], []
    for i, d in enumerate(devices):
        p, sec = divmod(i, n_section)
        if d.core_on_chip != core_of[sec] or where[(*d.coords, 1 - d.core_on_chip)] != p * n_section + partner_of[sec]:
            return None
        step = 1 if core_of[sec] == 0 else -1
        along.append((i, ((p + step) % n_pos) * n_section + sec))
        across.append((i, p * n_section + partner_of[sec]))
    return along, across, core_of, partner_of


def exchanged_halos(runs_of, widen, routes, my_section):
    along, across, core_of, partner_of = routes
    ring = ("pos", "section")
    group, channels = runs_of.shape[2], runs_of.shape[3]
    core = jnp.asarray(core_of, jnp.int32)[my_section]
    partner = jnp.asarray(partner_of, jnp.int32)[my_section]
    runs = widen // group
    classes = [lax.dynamic_index_in_dim(runs_of, c, axis=1, keepdims=False) for c in (my_section, partner)]
    tails = jnp.stack([c[-runs:].reshape(widen, channels) for c in classes])
    heads = jnp.stack([c[:runs].reshape(widen, channels) for c in classes])
    got = lax.ppermute(lax.select_n(core, tails, heads), ring, along)
    other = lax.ppermute(got[1], ring, across)
    return lax.select_n(core, got[0], other), lax.select_n(core, other, got[0])


def routed_weights(piece, routes, my_section):
    first, second = routes
    ring = ("pos", "section")
    across = lax.ppermute(piece, ring, first)
    held = [piece, across, lax.ppermute(piece, ring, second), lax.ppermute(across, ring, second)]
    picked = []
    for owner in range(len(held)):
        code = my_section ^ owner
        picked.append(lax.select_n((code & 1) * 2 + (code >> 1), *held))
    return jnp.stack(picked)


def from_shifts(piece, my_section):
    count = lax.axis_size("section")
    received = [piece] + [
        lax.ppermute(piece, "section", [(i, (i + hops) % count) for i in range(count)]) for hops in range(1, count)
    ]
    return jnp.stack(received)


def by_owner(received, my_section):
    count = received.shape[0]
    return jnp.stack(
        [lax.dynamic_index_in_dim(received, (my_section - owner) % count, keepdims=False) for owner in range(count)]
    )


def to_one_section(piece, target):
    count = lax.axis_size("section")
    return jnp.stack(
        [
            piece if source == target else lax.ppermute(piece, "section", [(source, target)])
            for source in range(count)
        ]
    )


def prepare(x, gain):
    r = x.astype(jnp.float32)
    meansq = jnp.mean(r * r, axis=-1, keepdims=True)
    return jax.nn.gelu(r * lax.rsqrt(meansq + 1e-06) * gain, approximate=False).astype(jnp.bfloat16)


def mix(x, before, h, after, taps, bias, mixing):
    conv = jnp.dot(h, taps[1], preferred_element_type=jnp.float32)
    conv = conv + jnp.dot(before, taps[0], preferred_element_type=jnp.float32)
    conv = conv + jnp.dot(after, taps[2], preferred_element_type=jnp.float32)
    g = jax.nn.gelu(conv + bias, approximate=False).astype(jnp.bfloat16)
    return (x.astype(jnp.float32) + jnp.dot(g, mixing, preferred_element_type=jnp.float32)).astype(jnp.bfloat16)


def widened_layer(x, gain, taps, bias, mixing, shift):
    count = x.shape[0]
    h = prepare(x, gain)
    return mix(
        x[shift : count - shift], h[: count - 2 * shift], h[shift : count - shift], h[2 * shift :], taps, bias, mixing
    )


def exchanged_layer(x, gain, taps, bias, mixing, shift):
    chunk = x.shape[0]
    h = prepare(x, gain)
    if shift % chunk == 0:
        before = shifted(h, shift // chunk)
        after = shifted(h, -(shift // chunk))
    else:
        before = jnp.concatenate([shifted(h[chunk - shift :], 1), h[: chunk - shift]], axis=0)
        after = jnp.concatenate([h[shift:], shifted(h[:shift], -1)], axis=0)
    return mix(x, before, h, after, taps, bias, mixing)


def body(routes, halos, sequence_features, norm_gain, conv_weight, conv_bias, mix_weight):
    n_section = lax.axis_size("section")
    my_section = lax.axis_index("section")
    per_section = conv_weight.shape[1]
    block, channels = sequence_features.shape
    first_dilation = block // 2 ** (per_section * n_section - 1)
    group = first_dilation // n_section
    runs = block // first_dilation

    matrices = jnp.concatenate(
        [
            conv_weight.reshape(1, per_section * 3, channels, channels),
            mix_weight.reshape(1, per_section, channels, channels),
        ],
        axis=1,
    )
    vectors = jnp.concatenate([norm_gain, conv_bias], axis=1)[0]

    runs_of = sequence_features.reshape(runs, n_section, group, channels)
    x = lax.dynamic_index_in_dim(runs_of, my_section, axis=1, keepdims=False).reshape(runs * group, channels)
    chunk = x.shape[0]

    shifts = [first_dilation * 2**index // n_section for index in range(per_section * n_section)]
    widen = sum(shifts[:REDUNDANT])
    assert widen <= chunk
    if halos is None or widen % group:
        x = jnp.concatenate([shifted(x[chunk - widen :], 1), x, shifted(x[:widen], -1)], axis=0)
    else:
        left, right = exchanged_halos(runs_of, widen, halos, my_section)
        x = jnp.concatenate([left, x, right], axis=0)

    n_matrix_rows = matrices.shape[1] * channels
    parts = exact_bf16_parts(vectors)
    filler = jnp.zeros((-parts.shape[0] % 16, channels), jnp.bfloat16)
    packed = jnp.concatenate([matrices[0].reshape(n_matrix_rows, channels), parts, filler], axis=0)
    if routes is None:
        packed = by_owner(from_shifts(packed, my_section), my_section)
    else:
        packed = routed_weights(packed, routes, my_section)
    matrices = packed[:, :n_matrix_rows].reshape(n_section, -1, channels, channels)
    parts = packed[:, n_matrix_rows : n_matrix_rows + parts.shape[0]].astype(jnp.float32)
    parts = parts.reshape(n_section, 3, -1, channels)
    vectors = parts[:, 0] + parts[:, 1] + parts[:, 2]

    outs = []
    for index, shift in enumerate(shifts):
        step, layer_index = divmod(index, per_section)
        params = (
            vectors[step, layer_index],
            matrices[step, 3 * layer_index : 3 * layer_index + 3],
            vectors[step, per_section + layer_index],
            matrices[step, 3 * per_section + layer_index],
            shift,
        )
        if index < REDUNDANT:
            x = widened_layer(x, *params)
        else:
            x = exchanged_layer(x, *params)
        if layer_index == per_section - 1:
            edge = (x.shape[0] - chunk) // 2
            outs.append(x[edge : edge + chunk])
    outs_here = jnp.stack(outs)
    sent = [
        lax.dynamic_index_in_dim(outs_here, (my_section + hops) % n_section, keepdims=False) for hops in range(n_section)
    ]
    sent = [sent[0]] + [
        lax.ppermute(sent[hops], "section", [(i, (i + hops) % n_section) for i in range(n_section)])
        for hops in range(1, n_section)
    ]
    result = by_owner(jnp.stack(sent), my_section)
    result = result.reshape(n_section, runs, group, channels).transpose(1, 0, 2, 3)
    return result.reshape(1, block, channels)


def solution(mesh):
    in_specs = (
        P("pos", None),
        P("section", None, None),
        P("section", None, None, None, None),
        P("section", None, None),
        P("section", None, None, None),
    )
    out_specs = P("section", "pos", None)
    routes = weight_routes(mesh) if mesh.shape["section"] == 4 else None
    return jax.shard_map(
        functools.partial(body, routes, halo_routes(mesh)), mesh=mesh, in_specs=in_specs, out_specs=out_specs, check_vma=False
    )
```
